1024 devices in a mesh: ep: 64 (over y, z), et: 8 (over x_lo, core), rep: 2 (over x_hi).
Axes of the slice: x: 8 (x_hi: 2, x_lo: 4; x = x_hi * 4 + x_lo), y: 8, z: 8, core: 2. Of those that a mesh axis runs over, the one named last changes fastest.
Arguments:
- grad_out: bfloat16 [32768, 7168], P(('ep', 'rep'), 'et'), may hold values from -6 to 6
- combine: float32 [32768, 2], P(('ep', 'rep')), may hold values from 0.1 to 1
- routing: int32 [32768, 2], P(('ep', 'rep')), may hold values from 0 to 63, all different within a row; in each aligned block of 256 rows (0 to 255, 256 to 511, ...) at most 12 rows name the same one
- expert_down_matrix: bfloat16 [64, 7168, 1024], P('ep', 'et'), may hold values from -0.0625 to 0.0625
- gate_pre: bfloat16 [64, 2, 1024, 768], P('ep', 'rep', 'et'), may hold values from -6 to 6
- up_pre: bfloat16 [64, 2, 1024, 768], P('ep', 'rep', 'et'), may hold values from -6 to 6
Outputs:
- grad_gate: bfloat16 [64, 2, 1024, 768], P('ep', 'rep', 'et')
- up_projection_gradient: bfloat16 [64, 2, 1024, 768], P('ep', 'rep', 'et')
- grad_down: bfloat16 [64, 7168, 1024], P('ep', ('et', 'rep'))
The draws below stay inside these ranges and needn't reach their ends.
Inputs may be any that keep to these rules, and one draw needn't show every extreme that they name: `routing`: each row names 2 different experts. Among the 256 rows of one token group (aligned blocks), no expert is named more than 12 times, a bound that some block reaches.
All inputs are finite; a program needn't handle non-finite values.
Results may differ from the reference program's by a relative error of at most 0.015.
Values may be sent and summed in bfloat16 or wider, within the bound.
No kernel may reach another device: no remote copies, remote signals or barrier semaphores. Data moves between devices by JAX's collectives and lax.ppermute only.
A program may use at most 32 MiB of HBM per device.

```python
import math
import jax
import jax.numpy as jnp
import numpy as np
from jax import lax

D = 7168
FF = 1024
TOPW = 2
GROUP_TOKENS = 256
CAP = 12
SLOTS = 768
TOKENS = 32768
N_EP = 64
N_ET = 8
N_REP = 2


def block_scale(key, dims, split, low, top_value):
    level = 1.0
    for axis_at, parts in split:
        steps = jax.random.uniform(jax.random.fold_in(jax.random.fold_in(key, 6), axis_at), (parts,), jnp.float32, low / len(split), top_value / len(split))
        level = level * jnp.repeat(jnp.exp(steps), dims[axis_at] // parts).reshape((-1,) + (1,) * (len(dims) - 1 - axis_at))
    return level


def assign_block(stream_key, own, number, rows, count, top, limit, lean):
    order = jax.random.permutation(stream_key, count)
    heavy_load, usual = portions_of(count, rows * top, limit, lean, True), portions_of(count, rows * top, limit, lean, False)
    places = jnp.arange(count)

    def named(lengths, offset_by):
        used = int((lengths > 0).sum())
        fixed = max(1, used // 4)
        passed = fixed + (places - fixed + offset_by * (used - fixed)) % max(1, count - fixed)
        return jnp.zeros((count,), jnp.int32).at[order[jnp.where(places < fixed, places, passed)]].set(jnp.asarray(lengths, jnp.int32))

    lengths = jnp.where(number % 4 == 0, named(heavy_load, number // 4), named(usual, number - number // 4 - 1))
    mixed = jax.random.permutation(jax.random.fold_in(own, 3), count)
    source_of, receiver = mixed[0:count // 2 * 2:2], mixed[1:count // 2 * 2:2]
    room = jnp.minimum(lengths[source_of] - 1, limit - lengths[receiver]) // 2
    room = jnp.where((source_of == order[0]) | (receiver == order[0]) | (lengths[receiver] == 0), 0, jnp.maximum(room, 0))
    passed = jax.random.randint(jax.random.fold_in(own, 4), (count // 2,), 0, 1 << 20) % (room + 1)
    lengths = lengths.at[source_of].add(-passed).at[receiver].add(passed)
    members = jnp.searchsorted(jnp.cumsum(lengths), jnp.arange(rows * top), side="right").astype(jnp.int32)
    listing = members.reshape(top, rows).T
    listing = listing[jax.random.permutation(jax.random.fold_in(own, 1), rows)]
    offset_by = jax.random.randint(jax.random.fold_in(own, 2), (rows, 1), 0, top)
    return jnp.take_along_axis(listing, (jnp.arange(top)[None, :] + offset_by) % top, axis=1)


def portions_of(number_of, total, reach, lean, full):
    weights = [(1 << 20) // math.isqrt(rank ** lean) + 1 for rank in range(1, number_of + 1)]
    largest = reach if full else min(reach, max(-(-total // number_of), total * weights[0] // sum(weights)))
    least = 1 if total - largest >= number_of - 1 else 0
    given, surplus = [largest] + [least] * (number_of - 1), total - largest - least * (number_of - 1)
    while surplus > 0:
        free = [i for i in range(1, number_of) if given[i] < largest] or [i for i in range(1, number_of) if given[i] < reach]
        pool, left = sum([weights[i] for i in free]), surplus
        for i in free:
            addition = min(reach - given[i], max(1, left * weights[i] // pool), surplus)
            given[i] = given[i] + addition
            surplus = surplus - addition
    return np.array(given)


def scatter_about(stream_key, shape, spread, reach, split=(), held_as=jnp.bfloat16):
    array = jax.random.normal(stream_key, shape, jnp.float32) * spread
    if len(split) > 0:
        array = block_scale(stream_key, shape, split, -0.22, 0.18) * array
    return jnp.clip(array, min=-reach, max=reach).astype(held_as)


def setup_inputs(seed: int = 0) -> dict:
    splits = jax.random.split(jax.random.key(seed), 7)
    grad_out = scatter_about(splits[0], (TOKENS, D), 1.0, 6.0, ((0, 128), (1, 8)))
    combine = jnp.clip(jnp.exp(math.log(1.0) - 2.3025851 * jax.random.uniform(splits[1], (TOKENS, TOPW), jnp.float32) ** block_scale(splits[1], (TOKENS, TOPW), ((0, 128),), -0.2, 0.2)), 0.1, 1.0)
    routing_keys = jax.random.split(jax.random.fold_in(splits[2], 1), TOKENS // GROUP_TOKENS)
    routing_turns = jax.random.permutation(jax.random.fold_in(splits[2], 3), TOKENS // GROUP_TOKENS)
    routing = jax.vmap(lambda own, number: assign_block(jax.random.fold_in(splits[2], 2), own, number, GROUP_TOKENS, N_EP, TOPW, CAP, 2))(routing_keys, routing_turns).reshape((TOKENS, TOPW))
    expert_down_matrix = scatter_about(splits[3], (N_EP, D, FF), D ** -0.5, 0.0625, ((0, 64), (1, 8)))
    gate_pre = scatter_about(splits[4], (N_EP, N_REP, FF, SLOTS), 2.0, 6.0, ((0, 64), (1, 2), (2, 8)))
    up_pre = scatter_about(splits[5], (N_EP, N_REP, FF, SLOTS), 1.0, 6.0, ((0, 64), (1, 2), (2, 8)))
    return dict(grad_out=grad_out, combine=combine, routing=routing, expert_down_matrix=expert_down_matrix, gate_pre=gate_pre, up_pre=up_pre)


def reference(grad_out, combine, routing, expert_down_matrix, gate_pre, up_pre):
    groups = N_EP * N_REP
    pair_total = GROUP_TOKENS * TOPW
    pair_ids = routing.reshape(groups, pair_total)
    pair_weights = combine.reshape(groups, pair_total)
    token_rows = grad_out.reshape(groups, GROUP_TOKENS, D)
    slot_iota = jnp.arange(CAP, dtype=jnp.int32)
    pair_iota = jnp.arange(pair_total, dtype=jnp.int32)

    def one_expert(expert):
        is_mine = (pair_ids == expert).astype(jnp.int32)
        ranking = jnp.cumsum(is_mine, axis=1, dtype=jnp.int32) - is_mine
        position = jnp.where(is_mine == 1, ranking, -1)
        matches = position[:, None, :] == slot_iota[None, :, None]
        filled = jnp.any(matches, axis=2)
        pair_index = jnp.sum(jnp.where(matches, pair_iota[None, None, :], 0), axis=2, dtype=jnp.int32)
        token_index = pair_index // TOPW
        routing_pair_weight = jnp.take_along_axis(pair_weights, pair_index, axis=1)
        picked = jax.vmap(lambda block_rows, chosen: jnp.take(block_rows, chosen, axis=0))(token_rows, token_index)
        routed = (picked.astype(jnp.float32) * routing_pair_weight[:, :, None]).astype(jnp.bfloat16)
        routed = jnp.where(filled[:, :, None], routed, jnp.zeros((), jnp.bfloat16))
        routed = routed.reshape(N_EP, N_REP, CAP, D).transpose(1, 0, 2, 3).reshape(N_REP, SLOTS, D)
        down_weight_blocks = expert_down_matrix[expert].reshape(N_ET, D // N_ET, FF).astype(jnp.float32)
        token_row_blocks = routed.reshape(N_REP, SLOTS, N_ET, D // N_ET).astype(jnp.float32)
        partial_value_term = jnp.einsum('kla,egkl->keag', down_weight_blocks, token_row_blocks)
        act_grad = jnp.sum(partial_value_term.astype(jnp.bfloat16).astype(jnp.float32), axis=0)
        gate_activation_values = gate_pre[expert].astype(jnp.float32)
        up_vals = up_pre[expert].astype(jnp.float32)
        gate_sig = jax.nn.sigmoid(gate_activation_values)
        grad_gate = (act_grad * up_vals * gate_sig * (1.0 + gate_activation_values * (1.0 - gate_sig))).astype(jnp.bfloat16)
        up_projection_gradient = (act_grad * gate_activation_values * gate_sig).astype(jnp.bfloat16)
        activation = (gate_activation_values * gate_sig * up_vals).astype(jnp.bfloat16)
        replica_part = jnp.einsum('rsd,rfs->rdf', routed.astype(jnp.float32), activation.astype(jnp.float32))
        grad_down = jnp.sum(replica_part.astype(jnp.bfloat16).astype(jnp.float32), axis=0).astype(jnp.bfloat16)
        return grad_gate, up_projection_gradient, grad_down

    grad_gate, up_projection_gradient, grad_down = lax.map(one_expert, jnp.arange(N_EP, dtype=jnp.int32))
    return (grad_gate, up_projection_gradient, grad_down)
```

```python
import jax
import jax.numpy as jnp
from jax import lax
from jax.sharding import PartitionSpec as P


def local(grad_out, combine, routing, expert_down_matrix, gate_pre, up_pre):
    expert_count = lax.axis_size("ep")
    rep_count = lax.axis_size("rep")
    rep_index = lax.axis_index("rep")
    slot_count = gate_pre.shape[-1]
    capacity = slot_count // expert_count
    tok_rows, feat_cols = grad_out.shape
    pair_width = routing.shape[1]
    pair_total = tok_rows * pair_width

    gate_activation_values = gate_pre[0, 0].astype(jnp.float32)
    up_vals = up_pre[0, 0].astype(jnp.float32)
    gate_sig = jax.nn.sigmoid(gate_activation_values)
    activation = (gate_activation_values * gate_sig * up_vals).astype(jnp.bfloat16)
    activation, gate_pre, up_pre = lax.optimization_barrier((activation, gate_pre, up_pre))
    activation_all = lax.all_gather(activation, "et", axis=0, tiled=True)
    gate_activation_values = gate_pre[0, 0].astype(jnp.float32)
    up_vals = up_pre[0, 0].astype(jnp.float32)
    gate_sig = jax.nn.sigmoid(gate_activation_values)

    targets = routing.reshape(pair_total)
    onehot = (targets[:, None] == jnp.arange(expert_count, dtype=jnp.int32)[None, :]).astype(
        jnp.int32
    )
    ranking = jnp.sum(
        (jnp.cumsum(onehot, axis=0, dtype=jnp.int32) - onehot) * onehot, axis=1, dtype=jnp.int32
    )
    destination = targets * capacity + ranking
    matches = destination[None, :] == jnp.arange(slot_count, dtype=jnp.int32)[:, None]
    filled = jnp.any(matches, axis=1)
    source_pair = jnp.sum(
        jnp.where(matches, jnp.arange(pair_total, dtype=jnp.int32)[None, :], 0),
        axis=1,
        dtype=jnp.int32,
    )
    pair_weight = jnp.take(combine.reshape(pair_total), source_pair, axis=0)
    picked = jnp.take(grad_out, source_pair // pair_width, axis=0)
    outgoing = jnp.where(
        filled[:, None],
        (picked.astype(jnp.float32) * pair_weight[:, None]).astype(jnp.bfloat16),
        jnp.zeros((), jnp.bfloat16),
    )
    outgoing = outgoing.reshape(expert_count, capacity, feat_cols)
    incoming = lax.all_to_all(outgoing, "ep", split_axis=0, concat_axis=0, tiled=True).reshape(
        slot_count, feat_cols
    )

    half = feat_cols // rep_count
    away_rows = lax.dynamic_slice_in_dim(incoming, (1 - rep_index) * half, half, axis=1)
    own_rows = lax.dynamic_slice_in_dim(incoming, rep_index * half, half, axis=1)
    away_part = lax.dot_general(
        away_rows, activation_all, (((0,), (1,)), ((), ())), preferred_element_type=jnp.float32
    ).astype(jnp.bfloat16)
    received = lax.ppermute(away_part, "rep", [(0, 1), (1, 0)])

    weight_rows = expert_down_matrix[0]
    act_grad = lax.psum_scatter(
        lax.dot_general(
            weight_rows, incoming, (((0,), (1,)), ((), ())), preferred_element_type=jnp.float32
        ).astype(jnp.bfloat16),
        "et",
        scatter_dimension=0,
        tiled=True,
    ).astype(jnp.float32)
    grad_gate = (
        act_grad * up_vals * gate_sig * (1.0 + gate_activation_values * (1.0 - gate_sig))
    ).astype(jnp.bfloat16)
    up_projection_gradient = (act_grad * gate_activation_values * gate_sig).astype(jnp.bfloat16)

    own_part = lax.dot_general(
        own_rows, activation_all, (((0,), (1,)), ((), ())), preferred_element_type=jnp.float32
    ).astype(jnp.bfloat16)
    grad_down = (own_part.astype(jnp.float32) + received.astype(jnp.float32)).astype(jnp.bfloat16)
    return (grad_gate[None, None], up_projection_gradient[None, None], grad_down[None])


def solution(mesh):
    return jax.shard_map(
        local,
        mesh=mesh,
        in_specs=(
            P(("ep", "rep"), "et"),
            P(("ep", "rep"), None),
            P(("ep", "rep"), None),
            P("ep", "et", None),
            P("ep", "rep", "et", None),
            P("ep", "rep", "et", None),
        ),
        out_specs=(
            P("ep", "rep", "et", None),
            P("ep", "rep", "et", None),
            P("ep", ("et", "rep"), None),
        ),
        check_vma=False,
    )
```

```python
import jax
import jax.numpy as jnp
from jax import lax
from jax.sharding import PartitionSpec as P


def local(grad_out, combine, routing, expert_down_matrix, gate_pre, up_pre):
    expert_count = lax.axis_size("ep")
    rep_count = lax.axis_size("rep")
    rep_index = lax.axis_index("rep")
    slot_count = gate_pre.shape[-1]
    capacity = slot_count // expert_count
    tok_rows, feat_cols = grad_out.shape
    pair_width = routing.shape[1]
    pair_total = tok_rows * pair_width

    gate_activation_values = gate_pre[0, 0].astype(jnp.float32)
    up_vals = up_pre[0, 0].astype(jnp.float32)
    gate_sig = jax.nn.sigmoid(gate_activation_values)
    activation = (gate_activation_values * gate_sig * up_vals).astype(jnp.bfloat16)
    activation, gate_pre, up_pre = lax.optimization_barrier((activation, gate_pre, up_pre))
    activation_all = lax.all_gather(activation, "et", axis=0, tiled=True)
    gate_activation_values = gate_pre[0, 0].astype(jnp.float32)
    up_vals = up_pre[0, 0].astype(jnp.float32)
    gate_sig = jax.nn.sigmoid(gate_activation_values)

    targets = routing.reshape(pair_total)
    onehot = (targets[:, None] == jnp.arange(expert_count, dtype=jnp.int32)[None, :]).astype(
        jnp.int32
    )
    ranking = jnp.sum(
        (jnp.cumsum(onehot, axis=0, dtype=jnp.int32) - onehot) * onehot, axis=1, dtype=jnp.int32
    )
    destination = targets * capacity + ranking
    matches = destination[None, :] == jnp.arange(slot_count, dtype=jnp.int32)[:, None]
    token_hit = jnp.any(matches.reshape(slot_count, tok_rows, pair_width), axis=2).astype(jnp.bfloat16)
    pair_weight = jnp.sum(
        jnp.where(matches, combine.reshape(pair_total)[None, :], 0.0), axis=1, dtype=jnp.float32
    )

    def routed(cols):
        picked = lax.dot_general(
            token_hit, cols, (((1,), (0,)), ((), ())), preferred_element_type=jnp.float32
        )
        rows = (picked * pair_weight[:, None]).astype(jnp.bfloat16)
        rows = rows.reshape(expert_count, capacity, cols.shape[1])
        sent = lax.all_to_all(rows, "ep", split_axis=0, concat_axis=0, tiled=True)
        return sent.reshape(slot_count, cols.shape[1])

    half = feat_cols // rep_count
    away_at = (1 - rep_index) * half
    own_at = rep_index * half
    away_rows = routed(lax.dynamic_slice_in_dim(grad_out, away_at, half, axis=1))
    away_part = lax.dot_general(
        away_rows, activation_all, (((0,), (1,)), ((), ())), preferred_element_type=jnp.float32
    ).astype(jnp.bfloat16)
    received = lax.ppermute(away_part, "rep", [(0, 1), (1, 0)])
    own_rows = routed(lax.dynamic_slice_in_dim(grad_out, own_at, half, axis=1))

    weight_rows = expert_down_matrix[0]
    block_sum = lax.dot_general(
        lax.dynamic_slice_in_dim(weight_rows, away_at, half, axis=0),
        away_rows,
        (((0,), (1,)), ((), ())),
        preferred_element_type=jnp.float32,
    ) + lax.dot_general(
        lax.dynamic_slice_in_dim(weight_rows, own_at, half, axis=0),
        own_rows,
        (((0,), (1,)), ((), ())),
        preferred_element_type=jnp.float32,
    )
    act_grad = lax.psum_scatter(
        block_sum.astype(jnp.bfloat16),
        "et",
        scatter_dimension=0,
        tiled=True,
    ).astype(jnp.float32)
    grad_gate = (
        act_grad * up_vals * gate_sig * (1.0 + gate_activation_values * (1.0 - gate_sig))
    ).astype(jnp.bfloat16)
    up_projection_gradient = (act_grad * gate_activation_values * gate_sig).astype(jnp.bfloat16)

    own_part = lax.dot_general(
        own_rows, activation_all, (((0,), (1,)), ((), ())), preferred_element_type=jnp.float32
    ).astype(jnp.bfloat16)
    grad_down = (own_part.astype(jnp.float32) + received.astype(jnp.float32)).astype(jnp.bfloat16)
    return (grad_gate[None, None], up_projection_gradient[None, None], grad_down[None])


def solution(mesh):
    return jax.shard_map(
        local,
        mesh=mesh,
        in_specs=(
            P(("ep", "rep"), "et"),
            P(("ep", "rep"), None),
            P(("ep", "rep"), None),
            P("ep", "et", None),
            P("ep", "rep", "et", None),
            P("ep", "rep", "et", None),
        ),
        out_specs=(
            P("ep", "rep", "et", None),
            P("ep", "rep", "et", None),
            P("ep", ("et", "rep"), None),
        ),
        check_vma=False,
    )
```

```python
import jax
import jax.numpy as jnp
from jax import lax
from jax.sharding import PartitionSpec as P


def scatter_sum_et(part):
    et_count = lax.axis_size("et")
    et_index = lax.axis_index("et")
    rows = part.shape[0] // et_count
    acc = part.reshape(et_count, rows, part.shape[1])
    step = 1
    while step < et_count:
        groups = acc.reshape(acc.shape[0] // 2, 2, rows, part.shape[1])
        bit = (et_index // step) % 2
        keep = lax.dynamic_index_in_dim(groups, bit, axis=1, keepdims=False)
        away = lax.dynamic_index_in_dim(groups, 1 - bit, axis=1, keepdims=False)
        got = lax.ppermute(
            away.astype(jnp.bfloat16), "et", [(i, i ^ step) for i in range(et_count)]
        )
        acc = keep.astype(jnp.float32) + got.astype(jnp.float32)
        step *= 2
    return acc[0]


def send_to_partner(block):
    et_count = lax.axis_size("et")
    rep_count = lax.axis_size("rep")
    far = et_count // 2

    def linear(et, rep):
        return et * rep_count + rep

    across = [
        (linear(et, rep), linear(et ^ far, rep ^ 1)) for et in range(et_count) for rep in range(rep_count)
    ]
    along = [(et, et ^ far) for et in range(et_count)]
    first, second = jnp.split(block, 2, axis=0)
    first_hop = lax.ppermute(first, "et", along)
    second_hop = lax.ppermute(second, ("et", "rep"), across)
    first_got = lax.ppermute(first_hop, ("et", "rep"), across)
    second_got = lax.ppermute(second_hop, "et", along)
    return jnp.concatenate([first_got, second_got], axis=0)


def local(grad_out, combine, routing, expert_down_matrix, gate_pre, up_pre):
    expert_count = lax.axis_size("ep")
    rep_count = lax.axis_size("rep")
    rep_index = lax.axis_index("rep")
    slot_count = gate_pre.shape[-1]
    capacity = slot_count // expert_count
    tok_rows, feat_cols = grad_out.shape
    pair_width = routing.shape[1]
    pair_total = tok_rows * pair_width

    gate_activation_values = gate_pre[0, 0].astype(jnp.float32)
    up_vals = up_pre[0, 0].astype(jnp.float32)
    gate_sig = jax.nn.sigmoid(gate_activation_values)
    activation = (gate_activation_values * gate_sig * up_vals).astype(jnp.bfloat16)
    activation, gate_pre, up_pre = lax.optimization_barrier((activation, gate_pre, up_pre))
    activation_all = lax.all_gather(activation, "et", axis=0, tiled=True)
    gate_activation_values = gate_pre[0, 0].astype(jnp.float32)
    up_vals = up_pre[0, 0].astype(jnp.float32)
    gate_sig = jax.nn.sigmoid(gate_activation_values)

    targets = routing.reshape(pair_total)
    onehot = (targets[:, None] == jnp.arange(expert_count, dtype=jnp.int32)[None, :]).astype(
        jnp.int32
    )
    ranking = jnp.sum(
        (jnp.cumsum(onehot, axis=0, dtype=jnp.int32) - onehot) * onehot, axis=1, dtype=jnp.int32
    )
    destination = targets * capacity + ranking
    matches = destination[None, :] == jnp.arange(slot_count, dtype=jnp.int32)[:, None]
    token_hit = jnp.any(matches.reshape(slot_count, tok_rows, pair_width), axis=2).astype(jnp.bfloat16)
    pair_weight = jnp.sum(
        jnp.where(matches, combine.reshape(pair_total)[None, :], 0.0), axis=1, dtype=jnp.float32
    )

    def routed(cols):
        picked = lax.dot_general(
            token_hit, cols, (((1,), (0,)), ((), ())), preferred_element_type=jnp.float32
        )
        rows = (picked * pair_weight[:, None]).astype(jnp.bfloat16)
        rows = rows.reshape(expert_count, capacity, cols.shape[1])
        sent = lax.all_to_all(rows, "ep", split_axis=0, concat_axis=0, tiled=True)
        return sent.reshape(slot_count, cols.shape[1])

    half = feat_cols // rep_count
    away_at = (1 - rep_index) * half
    own_at = rep_index * half
    away_rows = routed(lax.dynamic_slice_in_dim(grad_out, away_at, half, axis=1))
    away_part = lax.dot_general(
        away_rows, activation_all, (((0,), (1,)), ((), ())), preferred_element_type=jnp.float32
    ).astype(jnp.bfloat16)
    received = send_to_partner(away_part)
    own_rows = routed(lax.dynamic_slice_in_dim(grad_out, own_at, half, axis=1))

    weight_rows = expert_down_matrix[0]
    away_sum = lax.dot_general(
        lax.dynamic_slice_in_dim(weight_rows, away_at, half, axis=0),
        away_rows,
        (((0,), (1,)), ((), ())),
        preferred_element_type=jnp.float32,
    )
    block_sum = away_sum + lax.dot_general(
        lax.dynamic_slice_in_dim(weight_rows, own_at, half, axis=0),
        own_rows,
        (((0,), (1,)), ((), ())),
        preferred_element_type=jnp.float32,
    )
    act_grad = scatter_sum_et(block_sum.astype(jnp.bfloat16))
    grad_gate = (
        act_grad * up_vals * gate_sig * (1.0 + gate_activation_values * (1.0 - gate_sig))
    ).astype(jnp.bfloat16)
    up_projection_gradient = (act_grad * gate_activation_values * gate_sig).astype(jnp.bfloat16)

    own_part = lax.dot_general(
        own_rows, activation_all, (((0,), (1,)), ((), ())), preferred_element_type=jnp.float32
    ).astype(jnp.bfloat16)
    grad_down = (own_part.astype(jnp.float32) + received.astype(jnp.float32)).astype(jnp.bfloat16)
    return (grad_gate[None, None], up_projection_gradient[None, None], grad_down[None])


def solution(mesh):
    return jax.shard_map(
        local,
        mesh=mesh,
        in_specs=(
            P(("ep", "rep"), "et"),
            P(("ep", "rep"), None),
            P(("ep", "rep"), None),
            P("ep", "et", None),
            P("ep", "rep", "et", None),
            P("ep", "rep", "et", None),
        ),
        out_specs=(
            P("ep", "rep", "et", None),
            P("ep", "rep", "et", None),
            P("ep", ("et", "rep"), None),
        ),
        check_vma=False,
    )
```

```python
import jax
import jax.numpy as jnp
from jax import lax
from jax.sharding import PartitionSpec as P


def scatter_sum_et(part):
    et_count = lax.axis_size("et")
    et_index = lax.axis_index("et")
    rows = part.shape[0] // et_count
    acc = part.reshape(et_count, rows, part.shape[1])
    step = 1
    while step < et_count:
        groups = acc.reshape(acc.shape[0] // 2, 2, rows, part.shape[1])
        bit = (et_index // step) % 2
        keep = lax.dynamic_index_in_dim(groups, bit, axis=1, keepdims=False)
        away = lax.dynamic_index_in_dim(groups, 1 - bit, axis=1, keepdims=False)
        got = lax.ppermute(
            away.astype(jnp.bfloat16), "et", [(i, i ^ step) for i in range(et_count)]
        )
        acc = keep.astype(jnp.float32) + got.astype(jnp.float32)
        step *= 2
    return acc[0]


def local(grad_out, combine, routing, expert_down_matrix, gate_pre, up_pre):
    expert_count = lax.axis_size("ep")
    rep_count = lax.axis_size("rep")
    rep_index = lax.axis_index("rep")
    slot_count = gate_pre.shape[-1]
    capacity = slot_count // expert_count
    tok_rows, feat_cols = grad_out.shape
    pair_width = routing.shape[1]
    pair_total = tok_rows * pair_width

    gate_activation_values = gate_pre[0, 0].astype(jnp.float32)
    up_vals = up_pre[0, 0].astype(jnp.float32)
    gate_sig = jax.nn.sigmoid(gate_activation_values)
    activation = (gate_activation_values * gate_sig * up_vals).astype(jnp.bfloat16)
    activation, gate_pre, up_pre = lax.optimization_barrier((activation, gate_pre, up_pre))
    activation_all = lax.all_gather(activation, "et", axis=0, tiled=True)
    gate_activation_values = gate_pre[0, 0].astype(jnp.float32)
    up_vals = up_pre[0, 0].astype(jnp.float32)
    gate_sig = jax.nn.sigmoid(gate_activation_values)

    targets = routing.reshape(pair_total)
    onehot = (targets[:, None] == jnp.arange(expert_count, dtype=jnp.int32)[None, :]).astype(
        jnp.int32
    )
    ranking = jnp.sum(
        (jnp.cumsum(onehot, axis=0, dtype=jnp.int32) - onehot) * onehot, axis=1, dtype=jnp.int32
    )
    destination = targets * capacity + ranking
    matches = destination[None, :] == jnp.arange(slot_count, dtype=jnp.int32)[:, None]
    token_hit = jnp.any(matches.reshape(slot_count, tok_rows, pair_width), axis=2).astype(jnp.bfloat16)
    pair_weight = jnp.sum(
        jnp.where(matches, combine.reshape(pair_total)[None, :], 0.0), axis=1, dtype=jnp.float32
    )

    def routed(cols):
        picked = lax.dot_general(
            token_hit, cols, (((1,), (0,)), ((), ())), preferred_element_type=jnp.float32
        )
        rows = (picked * pair_weight[:, None]).astype(jnp.bfloat16)
        rows = rows.reshape(expert_count, capacity, cols.shape[1])
        sent = lax.all_to_all(rows, "ep", split_axis=0, concat_axis=0, tiled=True)
        return sent.reshape(slot_count, cols.shape[1])

    half = feat_cols // rep_count
    away_at = (1 - rep_index) * half
    own_at = rep_index * half
    away_rows = routed(lax.dynamic_slice_in_dim(grad_out, away_at, half, axis=1))
    away_part = lax.dot_general(
        away_rows, activation_all, (((0,), (1,)), ((), ())), preferred_element_type=jnp.float32
    ).astype(jnp.bfloat16)
    first, second = jnp.split(away_part, 2, axis=0)
    first_got = lax.ppermute(first, "rep", [(0, 1), (1, 0)])
    swapped = lax.all_to_all(
        jnp.broadcast_to(second[None], (rep_count,) + second.shape), "rep", 0, 0, tiled=True
    )
    second_got = lax.dynamic_index_in_dim(swapped, 1 - rep_index, axis=0, keepdims=False)
    received = jnp.concatenate([first_got, second_got], axis=0)
    own_rows = routed(lax.dynamic_slice_in_dim(grad_out, own_at, half, axis=1))

    weight_rows = expert_down_matrix[0]
    block_sum = lax.dot_general(
        lax.dynamic_slice_in_dim(weight_rows, away_at, half, axis=0),
        away_rows,
        (((0,), (1,)), ((), ())),
        preferred_element_type=jnp.float32,
    ) + lax.dot_general(
        lax.dynamic_slice_in_dim(weight_rows, own_at, half, axis=0),
        own_rows,
        (((0,), (1,)), ((), ())),
        preferred_element_type=jnp.float32,
    )
    act_grad = scatter_sum_et(block_sum.astype(jnp.bfloat16))
    grad_gate = (
        act_grad * up_vals * gate_sig * (1.0 + gate_activation_values * (1.0 - gate_sig))
    ).astype(jnp.bfloat16)
    up_projection_gradient = (act_grad * gate_activation_values * gate_sig).astype(jnp.bfloat16)

    own_part = lax.dot_general(
        own_rows, activation_all, (((0,), (1,)), ((), ())), preferred_element_type=jnp.float32
    ).astype(jnp.bfloat16)
    grad_down = (own_part.astype(jnp.float32) + received.astype(jnp.float32)).astype(jnp.bfloat16)
    return (grad_gate[None, None], up_projection_gradient[None, None], grad_down[None])


def solution(mesh):
    return jax.shard_map(
        local,
        mesh=mesh,
        in_specs=(
            P(("ep", "rep"), "et"),
            P(("ep", "rep"), None),
            P(("ep", "rep"), None),
            P("ep", "et", None),
            P("ep", "rep", "et", None),
            P("ep", "rep", "et", None),
        ),
        out_specs=(
            P("ep", "rep", "et", None),
            P("ep", "rep", "et", None),
            P("ep", ("et", "rep"), None),
        ),
        check_vma=False,
    )
```

```python
import jax
import jax.numpy as jnp
from jax import lax
from jax.sharding import PartitionSpec as P


def scatter_sum_et(part):
    et_count = lax.axis_size("et")
    et_index = lax.axis_index("et")
    rows = part.shape[0] // et_count
    acc = part.reshape(et_count, rows, part.shape[1])
    step = 1
    while step < et_count:
        groups = acc.reshape(acc.shape[0] // 2, 2, rows, part.shape[1])
        bit = (et_index // step) % 2
        keep = lax.dynamic_index_in_dim(groups, bit, axis=1, keepdims=False)
        away = lax.dynamic_index_in_dim(groups, 1 - bit, axis=1, keepdims=False)
        got = lax.ppermute(
            away.astype(jnp.bfloat16), "et", [(i, i ^ step) for i in range(et_count)]
        )
        total = keep.astype(jnp.float32) + got.astype(jnp.float32)
        step *= 2
        acc = total if step >= et_count else total.astype(jnp.bfloat16)
    return acc[0]


def local(grad_out, combine, routing, expert_down_matrix, gate_pre, up_pre):
    expert_count = lax.axis_size("ep")
    rep_count = lax.axis_size("rep")
    rep_index = lax.axis_index("rep")
    slot_count = gate_pre.shape[-1]
    capacity = slot_count // expert_count
    tok_rows, feat_cols = grad_out.shape
    pair_width = routing.shape[1]
    pair_total = tok_rows * pair_width

    gate_activation_values = gate_pre[0, 0].astype(jnp.float32)
    up_vals = up_pre[0, 0].astype(jnp.float32)
    gate_sig = jax.nn.sigmoid(gate_activation_values)
    activation = (gate_activation_values * gate_sig * up_vals).astype(jnp.bfloat16)
    activation, gate_pre, up_pre = lax.optimization_barrier((activation, gate_pre, up_pre))
    activation_all = lax.all_gather(activation, "et", axis=0, tiled=True)
    gate_activation_values = gate_pre[0, 0].astype(jnp.float32)
    up_vals = up_pre[0, 0].astype(jnp.float32)
    gate_sig = jax.nn.sigmoid(gate_activation_values)

    targets = routing.reshape(pair_total)
    onehot = (targets[:, None] == jnp.arange(expert_count, dtype=jnp.int32)[None, :]).astype(
        jnp.int32
    )
    ranking = jnp.sum(
        (jnp.cumsum(onehot, axis=0, dtype=jnp.int32) - onehot) * onehot, axis=1, dtype=jnp.int32
    )
    destination = targets * capacity + ranking
    matches = destination[None, :] == jnp.arange(slot_count, dtype=jnp.int32)[:, None]
    token_hit = jnp.any(matches.reshape(slot_count, tok_rows, pair_width), axis=2).astype(jnp.bfloat16)
    pair_weight = jnp.sum(
        jnp.where(matches, combine.reshape(pair_total)[None, :], 0.0), axis=1, dtype=jnp.float32
    )

    def routed(cols):
        picked = lax.dot_general(
            token_hit, cols, (((1,), (0,)), ((), ())), preferred_element_type=jnp.float32
        )
        rows = (picked * pair_weight[:, None]).astype(jnp.bfloat16)
        rows = rows.reshape(expert_count, capacity, cols.shape[1])
        sent = lax.all_to_all(rows, "ep", split_axis=0, concat_axis=0, tiled=True)
        return sent.reshape(slot_count, cols.shape[1])

    half = feat_cols // rep_count
    away_at = (1 - rep_index) * half
    own_at = rep_index * half
    away_rows = routed(lax.dynamic_slice_in_dim(grad_out, away_at, half, axis=1))
    away_part = lax.dot_general(
        away_rows, activation_all, (((0,), (1,)), ((), ())), preferred_element_type=jnp.float32
    ).astype(jnp.bfloat16)
    received = lax.ppermute(away_part, "rep", [(0, 1), (1, 0)])
    own_rows = routed(lax.dynamic_slice_in_dim(grad_out, own_at, half, axis=1))

    weight_rows = expert_down_matrix[0]
    block_sum = lax.dot_general(
        lax.dynamic_slice_in_dim(weight_rows, away_at, half, axis=0),
        away_rows,
        (((0,), (1,)), ((), ())),
        preferred_element_type=jnp.float32,
    ) + lax.dot_general(
        lax.dynamic_slice_in_dim(weight_rows, own_at, half, axis=0),
        own_rows,
        (((0,), (1,)), ((), ())),
        preferred_element_type=jnp.float32,
    )
    act_grad = scatter_sum_et(block_sum.astype(jnp.bfloat16))
    grad_gate = (
        act_grad * up_vals * gate_sig * (1.0 + gate_activation_values * (1.0 - gate_sig))
    ).astype(jnp.bfloat16)
    up_projection_gradient = (act_grad * gate_activation_values * gate_sig).astype(jnp.bfloat16)

    own_part = lax.dot_general(
        own_rows, activation_all, (((0,), (1,)), ((), ())), preferred_element_type=jnp.float32
    ).astype(jnp.bfloat16)
    grad_down = (own_part.astype(jnp.float32) + received.astype(jnp.float32)).astype(jnp.bfloat16)
    return (grad_gate[None, None], up_projection_gradient[None, None], grad_down[None])


def solution(mesh):
    return jax.shard_map(
        local,
        mesh=mesh,
        in_specs=(
            P(("ep", "rep"), "et"),
            P(("ep", "rep"), None),
            P(("ep", "rep"), None),
            P("ep", "et", None),
            P("ep", "rep", "et", None),
            P("ep", "rep", "et", None),
        ),
        out_specs=(
            P("ep", "rep", "et", None),
            P("ep", "rep", "et", None),
            P("ep", ("et", "rep"), None),
        ),
        check_vma=False,
    )
```

```python
import jax
import jax.numpy as jnp
from jax import lax
from jax.sharding import PartitionSpec as P


def scatter_sum_et(part):
    et_count = lax.axis_size("et")
    et_index = lax.axis_index("et")
    chips = et_count // 2
    chip = et_index // 2
    rows = part.shape[0] // et_count
    groups = part.reshape(chips, 2, rows, part.shape[1])
    core = et_index % 2
    keep = lax.dynamic_index_in_dim(groups, core, axis=1, keepdims=False)
    away = lax.dynamic_index_in_dim(groups, 1 - core, axis=1, keepdims=False)
    got = lax.ppermute(away, "et", [(i, i ^ 1) for i in range(et_count)])
    chip_sum = (keep.astype(jnp.float32) + got.astype(jnp.float32)).astype(jnp.bfloat16)
    total = lax.dynamic_index_in_dim(chip_sum, chip, axis=0, keepdims=False).astype(jnp.float32)
    for shift in range(1, chips):
        block = lax.dynamic_index_in_dim(chip_sum, (chip + shift) % chips, axis=0, keepdims=False)
        pairs = [(i, ((i // 2 + shift) % chips) * 2 + i % 2) for i in range(et_count)]
        total = total + lax.ppermute(block, "et", pairs).astype(jnp.float32)
    return total


def local(grad_out, combine, routing, expert_down_matrix, gate_pre, up_pre):
    expert_count = lax.axis_size("ep")
    rep_count = lax.axis_size("rep")
    rep_index = lax.axis_index("rep")
    slot_count = gate_pre.shape[-1]
    capacity = slot_count // expert_count
    tok_rows, feat_cols = grad_out.shape
    pair_width = routing.shape[1]
    pair_total = tok_rows * pair_width

    gate_activation_values = gate_pre[0, 0].astype(jnp.float32)
    up_vals = up_pre[0, 0].astype(jnp.float32)
    gate_sig = jax.nn.sigmoid(gate_activation_values)
    activation = (gate_activation_values * gate_sig * up_vals).astype(jnp.bfloat16)
    activation, gate_pre, up_pre = lax.optimization_barrier((activation, gate_pre, up_pre))
    activation_all = lax.all_gather(activation, "et", axis=0, tiled=True)
    gate_activation_values = gate_pre[0, 0].astype(jnp.float32)
    up_vals = up_pre[0, 0].astype(jnp.float32)
    gate_sig = jax.nn.sigmoid(gate_activation_values)

    targets = routing.reshape(pair_total)
    onehot = (targets[:, None] == jnp.arange(expert_count, dtype=jnp.int32)[None, :]).astype(
        jnp.int32
    )
    ranking = jnp.sum(
        (jnp.cumsum(onehot, axis=0, dtype=jnp.int32) - onehot) * onehot, axis=1, dtype=jnp.int32
    )
    destination = targets * capacity + ranking
    matches = destination[None, :] == jnp.arange(slot_count, dtype=jnp.int32)[:, None]
    token_hit = jnp.any(matches.reshape(slot_count, tok_rows, pair_width), axis=2).astype(jnp.bfloat16)
    pair_weight = jnp.sum(
        jnp.where(matches, combine.reshape(pair_total)[None, :], 0.0), axis=1, dtype=jnp.float32
    )

    def routed(cols):
        picked = lax.dot_general(
            token_hit, cols, (((1,), (0,)), ((), ())), preferred_element_type=jnp.float32
        )
        rows = (picked * pair_weight[:, None]).astype(jnp.bfloat16)
        rows = rows.reshape(expert_count, capacity, cols.shape[1])
        sent = lax.all_to_all(rows, "ep", split_axis=0, concat_axis=0, tiled=True)
        return sent.reshape(slot_count, cols.shape[1])

    half = feat_cols // rep_count
    away_at = (1 - rep_index) * half
    own_at = rep_index * half
    away_rows = routed(lax.dynamic_slice_in_dim(grad_out, away_at, half, axis=1))
    away_part = lax.dot_general(
        away_rows, activation_all, (((0,), (1,)), ((), ())), preferred_element_type=jnp.float32
    ).astype(jnp.bfloat16)
    received = lax.ppermute(away_part, "rep", [(0, 1), (1, 0)])
    own_rows = routed(lax.dynamic_slice_in_dim(grad_out, own_at, half, axis=1))

    weight_rows = expert_down_matrix[0]
    block_sum = lax.dot_general(
        lax.dynamic_slice_in_dim(weight_rows, away_at, half, axis=0),
        away_rows,
        (((0,), (1,)), ((), ())),
        preferred_element_type=jnp.float32,
    ) + lax.dot_general(
        lax.dynamic_slice_in_dim(weight_rows, own_at, half, axis=0),
        own_rows,
        (((0,), (1,)), ((), ())),
        preferred_element_type=jnp.float32,
    )
    act_grad = scatter_sum_et(block_sum.astype(jnp.bfloat16))
    grad_gate = (
        act_grad * up_vals * gate_sig * (1.0 + gate_activation_values * (1.0 - gate_sig))
    ).astype(jnp.bfloat16)
    up_projection_gradient = (act_grad * gate_activation_values * gate_sig).astype(jnp.bfloat16)

    own_part = lax.dot_general(
        own_rows, activation_all, (((0,), (1,)), ((), ())), preferred_element_type=jnp.float32
    ).astype(jnp.bfloat16)
    grad_down = (own_part.astype(jnp.float32) + received.astype(jnp.float32)).astype(jnp.bfloat16)
    return (grad_gate[None, None], up_projection_gradient[None, None], grad_down[None])


def solution(mesh):
    return jax.shard_map(
        local,
        mesh=mesh,
        in_specs=(
            P(("ep", "rep"), "et"),
            P(("ep", "rep"), None),
            P(("ep", "rep"), None),
            P("ep", "et", None),
            P("ep", "rep", "et", None),
            P("ep", "rep", "et", None),
        ),
        out_specs=(
            P("ep", "rep", "et", None),
            P("ep", "rep", "et", None),
            P("ep", ("et", "rep"), None),
        ),
        check_vma=False,
    )
```
